256 devices in a mesh: row: 16 (over z, y_lo), col: 16 (over y_hi, x, core).
Axes of the slice: x: 4, y: 4 (y_hi: 2, y_lo: 2; y = y_hi * 2 + y_lo), z: 8, core: 2. Of those that a mesh axis runs over, the one named last changes fastest.
Arguments:
- points: float32 [32, 65536], P(None, ('row', 'col')), may hold values from -6 to 6
- candidates: float32 [32, 16384], P(None, ('row', 'col')), may hold values from -6 to 6
- length_scales: float32 [32], replicated, may hold values from 1.5 to 4
- signal_var: float32 [1], replicated, may hold values from 0.5 to 2
- noise_var: float32 [1], replicated, may hold values from 0.1 to 1
- cand_prior: float32 [16384], P(('row', 'col')), may hold values from -6 to 6
- weights: float32 [16, 65536], P(None, ('row', 'col')), may hold values from -6 to 6
- residual: float32 [16, 65536], P(None, ('row', 'col')), may hold values from -300 to 300, as said below
- direction: float32 [16, 65536], P(None, ('row', 'col')), may hold values from -300 to 300, as said below
Outputs:
- weights_new: float32 [16, 65536], P(None, ('row', 'col'))
- residual_new: float32 [16, 65536], P(None, ('row', 'col'))
- direction_new: float32 [16, 65536], P(None, ('row', 'col'))
- cand_fit: float32 [16, 16384], P(None, ('row', 'col'))
The draws below stay inside these ranges and needn't reach their ends.
Inputs may be any that keep to these rules, and one draw needn't show every extreme that they name: `residual`: real values. `direction`: real values.
All inputs are finite; a program needn't handle non-finite values.
Results may differ from the reference program's by a relative error of at most 0.011.
Values may be sent and summed in bfloat16 or wider, within the bound.
No kernel may reach another device: no remote copies, remote signals or barrier semaphores. Data moves between devices by JAX's collectives and lax.ppermute only.
A program may use at most 64 MiB of HBM per device.

```python
import math
import jax
import jax.numpy as jnp
from jax import lax

F = 32
COLS = 16
N = 65536
Q = 16384


def rising_field(key, salt):
    key = jax.random.fold_in(key, salt)
    keys = jax.random.split(key, 3)
    positions = jnp.arange(N, dtype=jnp.float32)
    rising = jnp.exp(jnp.log(3.0) * positions / max(N - 1, 1))
    rough = jnp.exp(jnp.log(10.0) * jax.random.uniform(keys[0], (N,), jnp.float32))
    column_scale = jnp.exp(jnp.log(10.0) * jax.random.uniform(keys[1], (COLS, 1), jnp.float32))
    values = jax.random.truncated_normal(keys[2], -5.0, 5.0, (COLS, N), jnp.float32)
    return (values * rising[None, :] * rough[None, :] * column_scale / 10.0).astype(jnp.float32)


def draw_residual(key, part):
    return rising_field(key, 101)


def draw_direction(key, part):
    return rising_field(key, 202)


def steps_of(own_key, extent, shards, smallest, high):
    factor_of, own = 1.0, jax.random.fold_in(own_key, 6)
    for dim, blocks in shards:
        draws = jnp.exp(jax.random.uniform(jax.random.fold_in(own, dim), (blocks,), jnp.float32, smallest / len(shards), high / len(shards)))
        factor_of = factor_of * jnp.repeat(draws, extent[dim] // blocks).reshape([-1 if axis == dim else 1 for axis in range(len(extent))])
    return factor_of


def bell_draw(own_key, extent, spread, reach, cuts=(), kind=jnp.bfloat16):
    array = spread * jax.random.normal(own_key, extent, jnp.float32)
    if cuts:
        array = array * steps_of(own_key, extent, cuts, -0.22, 0.18)
    return jnp.clip(array, -reach, reach).astype(kind)


def setup_inputs(seed: int = 0) -> dict:
    splits = jax.random.split(jax.random.key(seed), 10)
    return {
        "points": bell_draw(splits[0], (F, N), 1.0, 6.0, ((1, 256),), jnp.float32),
        "candidates": bell_draw(splits[1], (F, Q), 1.0, 6.0, ((1, 256),), jnp.float32),
        "length_scales": jnp.clip(jnp.exp(jax.random.uniform(splits[2], (F,), jnp.float32, math.log(1.5), math.log(4.0))), 1.5, 4.0),
        "signal_var": jnp.clip(jnp.exp(jax.random.uniform(splits[3], (1,), jnp.float32, math.log(0.5), math.log(2.0))), 0.5, 2.0),
        "noise_var": jnp.clip(jnp.exp(jax.random.uniform(splits[4], (1,), jnp.float32, math.log(0.1), math.log(1.0))), 0.1, 1.0),
        "cand_prior": bell_draw(splits[5], (Q,), 1.0, 6.0, ((0, 256),), jnp.float32),
        "weights": bell_draw(splits[6], (COLS, N), 1.0, 6.0, ((1, 256),), jnp.float32),
        "residual": draw_residual(jax.random.fold_in(splits[9], 71), 0),
        "direction": draw_direction(jax.random.fold_in(splits[9], 71), 0),
    }


root_five = math.sqrt(5.0)
contract_first = (((0,), (0,)), ((), ()))
contract_last = (((1,), (1,)), ((), ()))

def square_norms(scaled):
    return lax.optimization_barrier(jnp.sum(jnp.square(scaled.astype(jnp.float32)), axis=0))

def matern_block(row_pts, row_sq, col_pts, col_sq, signal_scalar):
    inner_prod = lax.dot_general(row_pts, col_pts, contract_first, preferred_element_type=jnp.float32)
    dist_sq = jnp.maximum(row_sq[:, None] + col_sq[None, :] - 2.0 * inner_prod, 0.0)
    distance = jnp.sqrt(dist_sq)
    kern_vals = signal_scalar * (1.0 + root_five * distance + 5.0 / 3.0 * dist_sq) * jnp.exp(-root_five * distance)
    return kern_vals.astype(jnp.bfloat16)

def apply_rows(row_pts, col_pts, col_sq, vectors, signal_scalar):
    feature_count = row_pts.shape[0]
    row_count = row_pts.shape[1]
    block_len = math.gcd(row_count, 512)
    num_blocks = row_count // block_len
    blocks = row_pts.reshape(feature_count, num_blocks, block_len).transpose(1, 0, 2)

    def one_block(row_blk):
        kern_vals = matern_block(row_blk, square_norms(row_blk), col_pts, col_sq, signal_scalar)
        return lax.dot_general(vectors, kern_vals, contract_last, preferred_element_type=jnp.float32)
    result = lax.map(one_block, blocks)
    return result.transpose(1, 0, 2).reshape(vectors.shape[0], row_count)

def reference(points, candidates, length_scales, signal_var, noise_var, cand_prior, weights, residual, direction):
    scaled = (points / length_scales[:, None]).astype(jnp.bfloat16)
    cand_scaled = (candidates / length_scales[:, None]).astype(jnp.bfloat16)
    signal_scalar = signal_var[0]
    col_sq = square_norms(scaled)
    dir_low = direction.astype(jnp.bfloat16)
    kernel_out = apply_rows(scaled, scaled, col_sq, dir_low, signal_scalar)
    image_vec = kernel_out + noise_var[0] * direction
    norm_now = lax.optimization_barrier(jnp.sum(residual * residual, axis=1))
    curvature = lax.optimization_barrier(jnp.sum(direction * image_vec, axis=1))
    step_len = norm_now / curvature
    weights_new = weights + step_len[:, None] * direction
    residual_new = residual - step_len[:, None] * image_vec
    norm_next = lax.optimization_barrier(jnp.sum(residual_new * residual_new, axis=1))
    direction_new = residual_new + (norm_next / norm_now)[:, None] * direction
    w_low = weights_new.astype(jnp.bfloat16)
    fitted = apply_rows(cand_scaled, scaled, col_sq, w_low, signal_scalar)
    cand_fit = cand_prior[None, :] + fitted
    return (weights_new, residual_new, direction_new, cand_fit)
```

```python
import math

import jax
import jax.numpy as jnp
from jax import lax
from jax.sharding import PartitionSpec as P

root_five = math.sqrt(5.0)
contract_first = (((0,), (0,)), ((), ()))
contract_last = (((1,), (1,)), ((), ()))


def square_norms(scaled):
    return jnp.sum(jnp.square(scaled.astype(jnp.float32)), axis=0)


def matern_block(row_pts, row_sq, col_pts, col_sq, signal_scalar):
    inner_prod = lax.dot_general(
        row_pts, col_pts, contract_first, preferred_element_type=jnp.float32
    )
    dist_sq = jnp.maximum(row_sq[:, None] + col_sq[None, :] - 2.0 * inner_prod, 0.0)
    distance = jnp.sqrt(dist_sq)
    kern_vals = (
        signal_scalar
        * (1.0 + root_five * distance + 5.0 / 3.0 * dist_sq)
        * jnp.exp(-root_five * distance)
    )
    return kern_vals.astype(jnp.bfloat16)


def kernel_apply(row_pts, row_sq, col_pts, col_sq, vectors, signal_scalar, block_len):
    feature_count = col_pts.shape[0]
    num_blocks = col_pts.shape[1] // block_len
    pts_blocks = col_pts.reshape(feature_count, num_blocks, block_len).transpose(1, 0, 2)
    sq_blocks = col_sq.reshape(num_blocks, block_len)
    vec_blocks = vectors.reshape(vectors.shape[0], num_blocks, block_len).transpose(1, 0, 2)

    def one_block(total, pieces):
        pts_blk, sq_blk, vec_blk = pieces
        kern_vals = matern_block(row_pts, row_sq, pts_blk, sq_blk, signal_scalar)
        return (
            total
            + lax.dot_general(
                vec_blk, kern_vals, contract_last, preferred_element_type=jnp.float32
            ),
            None,
        )

    start = jnp.zeros((vectors.shape[0], row_pts.shape[1]), jnp.float32)
    result, ignored = lax.scan(one_block, start, (pts_blocks, sq_blocks, vec_blocks))
    return result


def xor_perm(size, bit):
    return [(i, i ^ (1 << bit)) for i in range(size)]


def gather_last(x, axis_name, size):
    me = lax.axis_index(axis_name)
    buf = x
    for bit in range(size.bit_length() - 1):
        recv = lax.ppermute(buf, axis_name, xor_perm(size, bit))
        low = ((me >> bit) & 1) == 0
        buf = jnp.where(
            low, jnp.concatenate([buf, recv], -1), jnp.concatenate([recv, buf], -1)
        )
    return buf


def reduce_scatter_last(x, axis_name, size):
    me = lax.axis_index(axis_name)
    buf = x
    for bit in reversed(range(size.bit_length() - 1)):
        half = buf.shape[-1] // 2
        lower, upper = buf[..., :half], buf[..., half:]
        low = ((me >> bit) & 1) == 0
        keep = jnp.where(low, lower, upper)
        send = jnp.where(low, upper, lower)
        buf = keep + lax.ppermute(send, axis_name, xor_perm(size, bit))
    return buf


def all_sum(x, axis_name, size):
    for bit in range(size.bit_length() - 1):
        x = x + lax.ppermute(x, axis_name, xor_perm(size, bit))
    return x


def per_device(
    points,
    candidates,
    length_scales,
    signal_var,
    noise_var,
    cand_prior,
    weights,
    residual,
    direction,
    n_row,
    n_col,
):
    scaled = (points / length_scales[:, None]).astype(jnp.bfloat16)
    cand_scaled = (candidates / length_scales[:, None]).astype(jnp.bfloat16)
    signal_scalar = signal_var[0]
    dir_low = direction.astype(jnp.bfloat16)
    cols, own = direction.shape
    own_cand = cand_scaled.shape[1]
    feats = scaled.shape[0]

    row_pack = gather_last(jnp.concatenate([scaled, cand_scaled], 1), "col", n_col)
    row_pack = row_pack.reshape(feats, n_col, own + own_cand)
    row_pts = row_pack[:, :, :own].reshape(feats, n_col * own)
    row_cands = row_pack[:, :, own:].reshape(feats, n_col * own_cand)
    col_pack = gather_last(jnp.concatenate([scaled, dir_low], 0), "row", n_row)
    col_pts = col_pack[:feats]
    col_dir = col_pack[feats:]
    row_state = gather_last(jnp.concatenate([residual, direction], 0), "col", n_col)
    res_row, dir_row = row_state[:cols], row_state[cols:]
    col_state = gather_last(jnp.concatenate([weights, direction], 0), "row", n_row)
    w_col, d_col = col_state[:cols], col_state[cols:]

    row_sq = square_norms(row_pts)
    col_sq = square_norms(col_pts)
    cand_sq = square_norms(row_cands)

    partial_rows = kernel_apply(
        row_pts, row_sq, col_pts, col_sq, col_dir, signal_scalar, 256
    )
    kernel_row = all_sum(partial_rows, "col", n_col)
    image_row = kernel_row + noise_var[0] * dir_row
    sums = all_sum(
        jnp.concatenate(
            [jnp.sum(res_row * res_row, axis=1), jnp.sum(dir_row * image_row, axis=1)]
        ),
        "row",
        n_row,
    )
    norm_now, curvature = sums[:cols], sums[cols:]
    step_len = norm_now / curvature
    residual_new_row = res_row - step_len[:, None] * image_row
    norm_next = all_sum(jnp.sum(residual_new_row * residual_new_row, axis=1), "row", n_row)

    me_col = lax.axis_index("col")
    image_vec = lax.dynamic_slice_in_dim(image_row, me_col * own, own, axis=1)
    weights_new = weights + step_len[:, None] * direction
    residual_new = residual - step_len[:, None] * image_vec
    direction_new = residual_new + (norm_next / norm_now)[:, None] * direction

    w_low_col = (w_col + step_len[:, None] * d_col).astype(jnp.bfloat16)
    partial_fit = kernel_apply(
        row_cands, cand_sq, col_pts, col_sq, w_low_col, signal_scalar, 1024
    )
    fitted = reduce_scatter_last(partial_fit, "col", n_col)
    cand_fit = cand_prior[None, :] + fitted
    return (weights_new, residual_new, direction_new, cand_fit)


def solution(mesh):
    placed = (
        P(None, ("row", "col")),
        P(None, ("row", "col")),
        P(),
        P(),
        P(),
        P(("row", "col")),
        P(None, ("row", "col")),
        P(None, ("row", "col")),
        P(None, ("row", "col")),
    )
    n_row, n_col = mesh.shape["row"], mesh.shape["col"]

    def body(*args):
        return per_device(*args, n_row=n_row, n_col=n_col)

    return jax.shard_map(
        body,
        mesh=mesh,
        in_specs=placed,
        out_specs=(
            P(None, ("row", "col")),
            P(None, ("row", "col")),
            P(None, ("row", "col")),
            P(None, ("row", "col")),
        ),
        check_vma=False,
    )
```

```python
import math

import jax
import jax.numpy as jnp
from jax import lax
from jax.sharding import PartitionSpec as P


root_five = math.sqrt(5.0)
contract_first = (((0,), (0,)), ((), ()))
contract_last = (((1,), (1,)), ((), ()))


def square_norms(scaled):
    return jnp.sum(jnp.square(scaled.astype(jnp.float32)), axis=0)


def matern_block(row_pts, row_sq, col_pts, col_sq, signal_scalar):
    inner_prod = lax.dot_general(
        row_pts, col_pts, contract_first, preferred_element_type=jnp.float32
    )
    dist_sq = jnp.maximum(row_sq[:, None] + col_sq[None, :] - 2.0 * inner_prod, 0.0)
    distance = jnp.sqrt(dist_sq)
    kern_vals = (
        signal_scalar
        * (1.0 + root_five * distance + 5.0 / 3.0 * dist_sq)
        * jnp.exp(-root_five * distance)
    )
    return kern_vals.astype(jnp.bfloat16)


def kernel_apply(row_pts, row_sq, col_pts, col_sq, vectors, signal_scalar, block_len):
    feature_count = col_pts.shape[0]
    num_blocks = col_pts.shape[1] // block_len
    pts_blocks = col_pts.reshape(feature_count, num_blocks, block_len).transpose(1, 0, 2)
    sq_blocks = col_sq.reshape(num_blocks, block_len)
    vec_blocks = vectors.reshape(vectors.shape[0], num_blocks, block_len).transpose(1, 0, 2)

    def one_block(total, pieces):
        pts_blk, sq_blk, vec_blk = pieces
        kern_vals = matern_block(row_pts, row_sq, pts_blk, sq_blk, signal_scalar)
        return (
            total
            + lax.dot_general(
                vec_blk, kern_vals, contract_last, preferred_element_type=jnp.float32
            ),
            None,
        )

    start = jnp.zeros((vectors.shape[0], row_pts.shape[1]), jnp.float32)
    result, _ = lax.scan(one_block, start, (pts_blocks, sq_blocks, vec_blocks))
    return result


def tied(x, dep):
    x, dep = lax.optimization_barrier((x, dep))
    return x


def xor_perm(size, bit):
    return [(i, i ^ (1 << bit)) for i in range(size)]


def gather_last(x, axis_name, size):
    me = lax.axis_index(axis_name)
    buf = x
    for bit in range(size.bit_length() - 1):
        recv = lax.ppermute(buf, axis_name, xor_perm(size, bit))
        low = ((me >> bit) & 1) == 0
        buf = jnp.where(
            low, jnp.concatenate([buf, recv], -1), jnp.concatenate([recv, buf], -1)
        )
    return buf


def reduce_scatter_last(x, axis_name, size):
    me = lax.axis_index(axis_name)
    buf = x
    for bit in reversed(range(size.bit_length() - 1)):
        half = buf.shape[-1] // 2
        lower, upper = buf[..., :half], buf[..., half:]
        low = ((me >> bit) & 1) == 0
        keep = jnp.where(low, lower, upper)
        send = jnp.where(low, upper, lower)
        buf = keep + lax.ppermute(send, axis_name, xor_perm(size, bit))
    return buf


def all_sum(x, axis_name, size):
    for bit in range(size.bit_length() - 1):
        x = x + lax.ppermute(x, axis_name, xor_perm(size, bit))
    return x


def per_device(
    points,
    candidates,
    length_scales,
    signal_var,
    noise_var,
    cand_prior,
    weights,
    residual,
    direction,
    n_row,
    n_col,
):
    scaled = (points / length_scales[:, None]).astype(jnp.bfloat16)
    cand_scaled = (candidates / length_scales[:, None]).astype(jnp.bfloat16)
    signal_scalar = signal_var[0]
    dir_low = direction.astype(jnp.bfloat16)
    cols, own = direction.shape
    own_cand = cand_scaled.shape[1]
    feats = scaled.shape[0]

    row_pack = gather_last(jnp.concatenate([scaled, cand_scaled], 1), "col", n_col)
    row_pack = row_pack.reshape(feats, n_col, own + own_cand)
    row_pts = row_pack[:, :, :own].reshape(feats, n_col * own)
    row_cands = row_pack[:, :, own:].reshape(feats, n_col * own_cand)
    col_pack = gather_last(jnp.concatenate([scaled, dir_low], 0), "row", n_row)
    col_pts = col_pack[:feats]
    col_dir = col_pack[feats:]
    row_state = gather_last(jnp.concatenate([residual, direction], 0), "col", n_col)
    res_row, dir_row = row_state[:cols], row_state[cols:]
    col_state = gather_last(jnp.concatenate([weights, direction], 0), "row", n_row)
    w_col, d_col = col_state[:cols], col_state[cols:]

    row_sq = square_norms(row_pts)
    col_sq = square_norms(col_pts)
    cand_sq = square_norms(row_cands)

    partial_rows = kernel_apply(
        row_pts, row_sq, col_pts, col_sq, col_dir, signal_scalar, 256
    )
    cand_blocks = []
    width = col_pts.shape[1] // 2
    for k in range(2):
        lo, hi = k * width, (k + 1) * width
        cand_blocks.append(
            lax.optimization_barrier(
                matern_block(
                    row_cands, cand_sq, col_pts[:, lo:hi], col_sq[lo:hi],
                    signal_scalar,
                )
            )
        )
    kernel_row = all_sum(partial_rows, "col", n_col)
    image_row = kernel_row + noise_var[0] * dir_row
    local_sums = jnp.concatenate(
        [jnp.sum(res_row * res_row, axis=1), jnp.sum(dir_row * image_row, axis=1)]
    )
    sums = all_sum(tied(local_sums, w_col), "row", n_row)
    norm_now, curvature = sums[:cols], sums[cols:]
    step_len = norm_now / curvature
    residual_new_row = res_row - step_len[:, None] * image_row

    me_col = lax.axis_index("col")
    image_vec = lax.dynamic_slice_in_dim(image_row, me_col * own, own, axis=1)
    weights_new = weights + step_len[:, None] * direction
    residual_new = residual - step_len[:, None] * image_vec

    w_low_col = (w_col + step_len[:, None] * d_col).astype(jnp.bfloat16)
    partial_fit = None
    for k in range(2):
        lo, hi = k * width, (k + 1) * width
        part = lax.dot_general(
            w_low_col[:, lo:hi], cand_blocks[k], contract_last,
            preferred_element_type=jnp.float32,
        )
        partial_fit = part if partial_fit is None else partial_fit + part
    norm_next = all_sum(
        tied(jnp.sum(residual_new_row * residual_new_row, axis=1), partial_fit),
        "row", n_row,
    )
    direction_new = residual_new + (norm_next / norm_now)[:, None] * direction
    fitted = reduce_scatter_last(partial_fit, "col", n_col)
    cand_fit = cand_prior[None, :] + fitted
    return (weights_new, residual_new, direction_new, cand_fit)


def solution(mesh):
    placed = (
        P(None, ("row", "col")),
        P(None, ("row", "col")),
        P(),
        P(),
        P(),
        P(("row", "col")),
        P(None, ("row", "col")),
        P(None, ("row", "col")),
        P(None, ("row", "col")),
    )
    n_row, n_col = mesh.shape["row"], mesh.shape["col"]

    def body(*args):
        return per_device(*args, n_row=n_row, n_col=n_col)

    return jax.shard_map(
        body,
        mesh=mesh,
        in_specs=placed,
        out_specs=(
            P(None, ("row", "col")),
            P(None, ("row", "col")),
            P(None, ("row", "col")),
            P(None, ("row", "col")),
        ),
        check_vma=False,
    )
```

```python
import math

import jax
import jax.numpy as jnp
from jax import lax
from jax.sharding import PartitionSpec as P


root_five = math.sqrt(5.0)
contract_first = (((0,), (0,)), ((), ()))
contract_last = (((1,), (1,)), ((), ()))


def square_norms(scaled):
    return jnp.sum(jnp.square(scaled.astype(jnp.float32)), axis=0)


def matern_block(row_pts, row_sq, col_pts, col_sq, signal_scalar):
    inner_prod = lax.dot_general(
        row_pts, col_pts, contract_first, preferred_element_type=jnp.float32
    )
    dist_sq = jnp.maximum(row_sq[:, None] + col_sq[None, :] - 2.0 * inner_prod, 0.0)
    distance = jnp.sqrt(dist_sq)
    kern_vals = (
        signal_scalar
        * (1.0 + root_five * distance + 5.0 / 3.0 * dist_sq)
        * jnp.exp(-root_five * distance)
    )
    return kern_vals.astype(jnp.bfloat16)


def kernel_apply(row_pts, row_sq, col_pts, col_sq, vectors, signal_scalar, block_len):
    feature_count = col_pts.shape[0]
    num_blocks = col_pts.shape[1] // block_len
    pts_blocks = col_pts.reshape(feature_count, num_blocks, block_len).transpose(1, 0, 2)
    sq_blocks = col_sq.reshape(num_blocks, block_len)
    vec_blocks = vectors.reshape(vectors.shape[0], num_blocks, block_len).transpose(1, 0, 2)

    def one_block(total, pieces):
        pts_blk, sq_blk, vec_blk = pieces
        kern_vals = matern_block(row_pts, row_sq, pts_blk, sq_blk, signal_scalar)
        return (
            total
            + lax.dot_general(
                vec_blk, kern_vals, contract_last, preferred_element_type=jnp.float32
            ),
            None,
        )

    start = jnp.zeros((vectors.shape[0], row_pts.shape[1]), jnp.float32)
    result, _ = lax.scan(one_block, start, (pts_blocks, sq_blocks, vec_blocks))
    return result


def tied(x, dep):
    x, dep = lax.optimization_barrier((x, dep))
    return x


def xor_perm(size, bit):
    return [(i, i ^ (1 << bit)) for i in range(size)]


def gather_last(x, axis_name, size):
    me = lax.axis_index(axis_name)
    buf = x
    for bit in range(size.bit_length() - 1):
        recv = lax.ppermute(buf, axis_name, xor_perm(size, bit))
        low = ((me >> bit) & 1) == 0
        buf = jnp.where(
            low, jnp.concatenate([buf, recv], -1), jnp.concatenate([recv, buf], -1)
        )
    return buf


def all_sum_grid(x, n_row, n_col):
    rounds = min(n_row, n_col).bit_length() - 1
    for bit in range(rounds):
        step = 1 << bit
        diag = [
            (r * n_col + c, (r ^ step) * n_col + (c ^ step))
            for r in range(n_row)
            for c in range(n_col)
        ]
        from_col = lax.ppermute(x, "col", xor_perm(n_col, bit))
        from_row = lax.ppermute(x, "row", xor_perm(n_row, bit))
        from_diag = lax.ppermute(x, ("row", "col"), diag)
        x = (x + from_col) + (from_row + from_diag)
    for bit in range(rounds, n_row.bit_length() - 1):
        x = x + lax.ppermute(x, "row", xor_perm(n_row, bit))
    for bit in range(rounds, n_col.bit_length() - 1):
        x = x + lax.ppermute(x, "col", xor_perm(n_col, bit))
    return x


def reduce_scatter_last(x, axis_name, size):
    me = lax.axis_index(axis_name)
    buf = x
    for bit in reversed(range(size.bit_length() - 1)):
        half = buf.shape[-1] // 2
        lower, upper = buf[..., :half], buf[..., half:]
        low = ((me >> bit) & 1) == 0
        keep = jnp.where(low, lower, upper)
        send = jnp.where(low, upper, lower)
        buf = keep + lax.ppermute(send, axis_name, xor_perm(size, bit))
    return buf


def all_sum(x, axis_name, size):
    for bit in range(size.bit_length() - 1):
        x = x + lax.ppermute(x, axis_name, xor_perm(size, bit))
    return x


def per_device(
    points,
    candidates,
    length_scales,
    signal_var,
    noise_var,
    cand_prior,
    weights,
    residual,
    direction,
    n_row,
    n_col,
):
    scaled = (points / length_scales[:, None]).astype(jnp.bfloat16)
    cand_scaled = (candidates / length_scales[:, None]).astype(jnp.bfloat16)
    signal_scalar = signal_var[0]
    cols, own = direction.shape
    own_cand = cand_scaled.shape[1]
    feats = scaled.shape[0]

    cand_rows = own_cand * feats // own
    row_pack = gather_last(
        jnp.concatenate(
            [
                scaled.astype(jnp.float32),
                cand_scaled.astype(jnp.float32).reshape(cand_rows, own),
                direction,
            ],
            0,
        ),
        "col",
        n_col,
    )
    row_pts = row_pack[:feats].astype(jnp.bfloat16)
    row_cands = (
        row_pack[feats:feats + cand_rows]
        .reshape(cand_rows, n_col, own)
        .transpose(1, 0, 2)
        .reshape(n_col, feats, own_cand)
        .transpose(1, 0, 2)
        .reshape(feats, n_col * own_cand)
        .astype(jnp.bfloat16)
    )
    dir_row = row_pack[feats + cand_rows:]
    col_pack = gather_last(
        jnp.concatenate([scaled.astype(jnp.float32), direction, weights], 0),
        "row",
        n_row,
    )
    col_pts = col_pack[:feats].astype(jnp.bfloat16)
    d_col = col_pack[feats:feats + cols]
    w_col = col_pack[feats + cols:]
    col_dir = d_col.astype(jnp.bfloat16)
    row_sq = square_norms(row_pts)
    col_sq = square_norms(col_pts)
    cand_sq = square_norms(row_cands)

    partial_rows = kernel_apply(
        row_pts, row_sq, col_pts, col_sq, col_dir, signal_scalar, 256
    )
    cand_blocks = []
    width = col_pts.shape[1] // 2
    for k in range(2):
        lo, hi = k * width, (k + 1) * width
        cand_blocks.append(
            lax.optimization_barrier(
                matern_block(
                    row_cands, cand_sq, col_pts[:, lo:hi], col_sq[lo:hi],
                    signal_scalar,
                )
            )
        )
    noise = noise_var[0]
    local_sums = jnp.concatenate(
        [
            jnp.sum(residual * residual, axis=1),
            jnp.sum(dir_row * partial_rows, axis=1)
            + noise * jnp.sum(direction * direction, axis=1),
        ]
    )
    sums = all_sum_grid(local_sums, n_row, n_col)
    kernel_row = all_sum(partial_rows, "col", n_col)
    norm_now, curvature = sums[:cols], sums[cols:]
    step_len = norm_now / curvature

    me_col = lax.axis_index("col")
    kernel_own = lax.dynamic_slice_in_dim(kernel_row, me_col * own, own, axis=1)
    image_vec = kernel_own + noise * direction
    weights_new = weights + step_len[:, None] * direction
    residual_new = residual - step_len[:, None] * image_vec

    w_low_col = (w_col + step_len[:, None] * d_col).astype(jnp.bfloat16)
    partial_fit = None
    for k in range(2):
        lo, hi = k * width, (k + 1) * width
        part = lax.dot_general(
            w_low_col[:, lo:hi], cand_blocks[k], contract_last,
            preferred_element_type=jnp.float32,
        )
        partial_fit = part if partial_fit is None else partial_fit + part
    norm_next = all_sum_grid(
        tied(jnp.sum(residual_new * residual_new, axis=1), partial_fit),
        n_row, n_col,
    )
    direction_new = residual_new + (norm_next / norm_now)[:, None] * direction
    fitted = reduce_scatter_last(partial_fit, "col", n_col)
    cand_fit = cand_prior[None, :] + fitted
    return (weights_new, residual_new, direction_new, cand_fit)


def solution(mesh):
    placed = (
        P(None, ("row", "col")),
        P(None, ("row", "col")),
        P(),
        P(),
        P(),
        P(("row", "col")),
        P(None, ("row", "col")),
        P(None, ("row", "col")),
        P(None, ("row", "col")),
    )
    n_row, n_col = mesh.shape["row"], mesh.shape["col"]

    def body(*args):
        return per_device(*args, n_row=n_row, n_col=n_col)

    return jax.shard_map(
        body,
        mesh=mesh,
        in_specs=placed,
        out_specs=(
            P(None, ("row", "col")),
            P(None, ("row", "col")),
            P(None, ("row", "col")),
            P(None, ("row", "col")),
        ),
        check_vma=False,
    )
```

```python
import math

import jax
import jax.numpy as jnp
from jax import lax
from jax.sharding import PartitionSpec as P


root_five = math.sqrt(5.0)
contract_first = (((0,), (0,)), ((), ()))
contract_last = (((1,), (1,)), ((), ()))


def square_norms(scaled):
    return jnp.sum(jnp.square(scaled.astype(jnp.float32)), axis=0)


def matern_block(row_pts, row_sq, col_pts, col_sq, signal_scalar):
    inner_prod = lax.dot_general(
        row_pts, col_pts, contract_first, preferred_element_type=jnp.float32
    )
    dist_sq = jnp.maximum(row_sq[:, None] + col_sq[None, :] - 2.0 * inner_prod, 0.0)
    distance = jnp.sqrt(dist_sq)
    kern_vals = (
        signal_scalar
        * (1.0 + root_five * distance + 5.0 / 3.0 * dist_sq)
        * jnp.exp(-root_five * distance)
    )
    return kern_vals.astype(jnp.bfloat16)


def kernel_apply(row_pts, row_sq, col_pts, col_sq, vectors, signal_scalar, block_len):
    feature_count = col_pts.shape[0]
    num_blocks = col_pts.shape[1] // block_len
    pts_blocks = col_pts.reshape(feature_count, num_blocks, block_len).transpose(1, 0, 2)
    sq_blocks = col_sq.reshape(num_blocks, block_len)
    vec_blocks = vectors.reshape(vectors.shape[0], num_blocks, block_len).transpose(1, 0, 2)

    def one_block(total, pieces):
        pts_blk, sq_blk, vec_blk = pieces
        kern_vals = matern_block(row_pts, row_sq, pts_blk, sq_blk, signal_scalar)
        return (
            total
            + lax.dot_general(
                vec_blk, kern_vals, contract_last, preferred_element_type=jnp.float32
            ),
            None,
        )

    start = jnp.zeros((vectors.shape[0], row_pts.shape[1]), jnp.float32)
    result, _ = lax.scan(one_block, start, (pts_blocks, sq_blocks, vec_blocks))
    return result


def tied(x, dep):
    x, dep = lax.optimization_barrier((x, dep))
    return x


def xor_perm(size, bit):
    return [(i, i ^ (1 << bit)) for i in range(size)]


def bit_reversed(index, nbits):
    out = 0
    for bit in range(nbits):
        out = out | (((index >> bit) & 1) << (nbits - 1 - bit))
    return out


def gather_last(x, axis_name, size):
    me = lax.axis_index(axis_name)
    buf = x
    for bit in reversed(range(size.bit_length() - 1)):
        recv = lax.ppermute(buf, axis_name, xor_perm(size, bit))
        low = ((me >> bit) & 1) == 0
        buf = jnp.where(
            low, jnp.concatenate([buf, recv], -1), jnp.concatenate([recv, buf], -1)
        )
    return buf


def reduce_scatter_last(x, axis_name, size):
    me = lax.axis_index(axis_name)
    buf = x
    for bit in range(size.bit_length() - 1):
        half = buf.shape[-1] // 2
        lower, upper = buf[..., :half], buf[..., half:]
        low = ((me >> bit) & 1) == 0
        keep = jnp.where(low, lower, upper)
        send = jnp.where(low, upper, lower)
        buf = keep + lax.ppermute(send, axis_name, xor_perm(size, bit))
    return buf


def all_sum(x, axis_name, size):
    for bit in range(size.bit_length() - 1):
        x = x + lax.ppermute(x, axis_name, xor_perm(size, bit))
    return x


def per_device(
    points,
    candidates,
    length_scales,
    signal_var,
    noise_var,
    cand_prior,
    weights,
    residual,
    direction,
    n_row,
    n_col,
):
    scaled = (points / length_scales[:, None]).astype(jnp.bfloat16)
    cand_scaled = (candidates / length_scales[:, None]).astype(jnp.bfloat16)
    signal_scalar = signal_var[0]
    dir_low = direction.astype(jnp.bfloat16)
    cols, own = direction.shape
    own_cand = cand_scaled.shape[1]
    feats = scaled.shape[0]

    row_pack = gather_last(jnp.concatenate([scaled, cand_scaled], 1), "col", n_col)
    row_pack = row_pack.reshape(feats, n_col, own + own_cand)
    row_pts = row_pack[:, :, :own].reshape(feats, n_col * own)
    row_cands = row_pack[:, :, own:].reshape(feats, n_col * own_cand)
    col_pack = gather_last(jnp.concatenate([scaled, dir_low], 0), "row", n_row)
    col_pts = col_pack[:feats]
    col_dir = col_pack[feats:]
    row_state = gather_last(jnp.concatenate([residual, direction], 0), "col", n_col)
    res_row, dir_row = row_state[:cols], row_state[cols:]
    col_state = gather_last(jnp.concatenate([weights, direction], 0), "row", n_row)
    w_col, d_col = col_state[:cols], col_state[cols:]

    row_sq = square_norms(row_pts)
    col_sq = square_norms(col_pts)
    cand_sq = square_norms(row_cands)

    partial_rows = kernel_apply(
        row_pts, row_sq, col_pts, col_sq, col_dir, signal_scalar, 256
    )
    cand_blocks = []
    width = col_pts.shape[1] // 2
    for k in range(2):
        lo, hi = k * width, (k + 1) * width
        cand_blocks.append(
            lax.optimization_barrier(
                matern_block(
                    row_cands, cand_sq, col_pts[:, lo:hi], col_sq[lo:hi],
                    signal_scalar,
                )
            )
        )
    kernel_row = all_sum(partial_rows, "col", n_col)
    image_row = kernel_row + noise_var[0] * dir_row
    local_sums = jnp.concatenate(
        [jnp.sum(res_row * res_row, axis=1), jnp.sum(dir_row * image_row, axis=1)]
    )
    sums = all_sum(tied(local_sums, w_col), "row", n_row)
    norm_now, curvature = sums[:cols], sums[cols:]
    step_len = norm_now / curvature
    residual_new_row = res_row - step_len[:, None] * image_row

    me_col = lax.axis_index("col")
    own_at = bit_reversed(me_col, n_col.bit_length() - 1) * own
    image_vec = lax.dynamic_slice_in_dim(image_row, own_at, own, axis=1)
    weights_new = weights + step_len[:, None] * direction
    residual_new = residual - step_len[:, None] * image_vec

    w_low_col = (w_col + step_len[:, None] * d_col).astype(jnp.bfloat16)
    partial_fit = None
    for k in range(2):
        lo, hi = k * width, (k + 1) * width
        part = lax.dot_general(
            w_low_col[:, lo:hi], cand_blocks[k], contract_last,
            preferred_element_type=jnp.float32,
        )
        partial_fit = part if partial_fit is None else partial_fit + part
    norm_next = all_sum(
        tied(jnp.sum(residual_new_row * residual_new_row, axis=1), partial_fit),
        "row", n_row,
    )
    direction_new = residual_new + (norm_next / norm_now)[:, None] * direction
    fitted = reduce_scatter_last(partial_fit, "col", n_col)
    cand_fit = cand_prior[None, :] + fitted
    return (weights_new, residual_new, direction_new, cand_fit)


def solution(mesh):
    placed = (
        P(None, ("row", "col")),
        P(None, ("row", "col")),
        P(),
        P(),
        P(),
        P(("row", "col")),
        P(None, ("row", "col")),
        P(None, ("row", "col")),
        P(None, ("row", "col")),
    )
    n_row, n_col = mesh.shape["row"], mesh.shape["col"]

    def body(*args):
        return per_device(*args, n_row=n_row, n_col=n_col)

    return jax.shard_map(
        body,
        mesh=mesh,
        in_specs=placed,
        out_specs=(
            P(None, ("row", "col")),
            P(None, ("row", "col")),
            P(None, ("row", "col")),
            P(None, ("row", "col")),
        ),
        check_vma=False,
    )
```

```python
import math

import jax
import jax.numpy as jnp
from jax import lax
from jax.sharding import PartitionSpec as P


root_five = math.sqrt(5.0)
contract_first = (((0,), (0,)), ((), ()))
contract_last = (((1,), (1,)), ((), ()))


def square_norms(scaled):
    return jnp.sum(jnp.square(scaled.astype(jnp.float32)), axis=0)


def matern_block(row_pts, row_sq, col_pts, col_sq, signal_scalar):
    inner_prod = lax.dot_general(
        row_pts, col_pts, contract_first, preferred_element_type=jnp.float32
    )
    dist_sq = jnp.maximum(row_sq[:, None] + col_sq[None, :] - 2.0 * inner_prod, 0.0)
    distance = jnp.sqrt(dist_sq)
    kern_vals = (
        signal_scalar
        * (1.0 + root_five * distance + 5.0 / 3.0 * dist_sq)
        * jnp.exp(-root_five * distance)
    )
    return kern_vals.astype(jnp.bfloat16)


def kernel_apply(row_pts, row_sq, col_pts, col_sq, vectors, signal_scalar, block_len):
    feature_count = col_pts.shape[0]
    num_blocks = col_pts.shape[1] // block_len
    pts_blocks = col_pts.reshape(feature_count, num_blocks, block_len).transpose(1, 0, 2)
    sq_blocks = col_sq.reshape(num_blocks, block_len)
    vec_blocks = vectors.reshape(vectors.shape[0], num_blocks, block_len).transpose(1, 0, 2)

    def one_block(total, pieces):
        pts_blk, sq_blk, vec_blk = pieces
        kern_vals = matern_block(row_pts, row_sq, pts_blk, sq_blk, signal_scalar)
        return (
            total
            + lax.dot_general(
                vec_blk, kern_vals, contract_last, preferred_element_type=jnp.float32
            ),
            None,
        )

    start = jnp.zeros((vectors.shape[0], row_pts.shape[1]), jnp.float32)
    result, _ = lax.scan(one_block, start, (pts_blocks, sq_blocks, vec_blocks))
    return result


def tied(x, dep):
    x, dep = lax.optimization_barrier((x, dep))
    return x


def xor_perm(size, bit):
    return [(i, i ^ (1 << bit)) for i in range(size)]


def bit_reversed(index, nbits):
    out = 0
    for bit in range(nbits):
        out = out | (((index >> bit) & 1) << (nbits - 1 - bit))
    return out


def gather_last(x, axis_name, size):
    me = lax.axis_index(axis_name)
    buf = x
    for bit in reversed(range(size.bit_length() - 1)):
        recv = lax.ppermute(buf, axis_name, xor_perm(size, bit))
        low = ((me >> bit) & 1) == 0
        buf = jnp.where(
            low, jnp.concatenate([buf, recv], -1), jnp.concatenate([recv, buf], -1)
        )
    return buf


def reduce_scatter_last(x, axis_name, size):
    me = lax.axis_index(axis_name)
    buf = x
    for bit in range(size.bit_length() - 1):
        half = buf.shape[-1] // 2
        lower, upper = buf[..., :half], buf[..., half:]
        low = ((me >> bit) & 1) == 0
        keep = jnp.where(low, lower, upper)
        send = jnp.where(low, upper, lower)
        buf = keep + lax.ppermute(send, axis_name, xor_perm(size, bit))
    return buf


def all_sum(x, axis_name, size):
    for bit in range(size.bit_length() - 1):
        x = x + lax.ppermute(x, axis_name, xor_perm(size, bit))
    return x


def per_device(
    points,
    candidates,
    length_scales,
    signal_var,
    noise_var,
    cand_prior,
    weights,
    residual,
    direction,
    n_row,
    n_col,
):
    scaled = (points / length_scales[:, None]).astype(jnp.bfloat16)
    cand_scaled = (candidates / length_scales[:, None]).astype(jnp.bfloat16)
    signal_scalar = signal_var[0]
    cols, own = direction.shape
    own_cand = cand_scaled.shape[1]
    feats = scaled.shape[0]

    def split(x):
        lo = x - lax.reduce_precision(x, exponent_bits=8, mantissa_bits=7)
        return x.astype(jnp.bfloat16), lo.astype(jnp.bfloat16)

    def join(hi, lo):
        return hi.astype(jnp.float32) + lo.astype(jnp.float32)

    dir_hi, dir_lo = split(direction)
    res_hi, res_lo = split(residual)
    w_hi, w_lo = split(weights)
    cand_rows = own_cand * feats // own
    row_pack = gather_last(
        jnp.concatenate(
            [scaled, cand_scaled.reshape(cand_rows, own), dir_hi, dir_lo, res_hi, res_lo],
            0,
        ),
        "col",
        n_col,
    )
    row_pts = row_pack[:feats]
    row_cands = (
        row_pack[feats:feats + cand_rows]
        .reshape(cand_rows, n_col, own)
        .transpose(1, 0, 2)
        .reshape(n_col, feats, own_cand)
        .transpose(1, 0, 2)
        .reshape(feats, n_col * own_cand)
    )
    at = feats + cand_rows
    dir_row = join(row_pack[at:at + cols], row_pack[at + cols:at + 2 * cols])
    at += 2 * cols
    res_row = join(row_pack[at:at + cols], row_pack[at + cols:at + 2 * cols])
    col_pack = gather_last(
        jnp.concatenate([scaled, dir_hi, dir_lo, w_hi, w_lo], 0), "row", n_row
    )
    col_pts = col_pack[:feats]
    col_dir = col_pack[feats:feats + cols]
    d_col = join(col_dir, col_pack[feats + cols:feats + 2 * cols])
    at = feats + 2 * cols
    w_col = join(col_pack[at:at + cols], col_pack[at + cols:at + 2 * cols])
    row_sq = square_norms(row_pts)
    col_sq = square_norms(col_pts)
    cand_sq = square_norms(row_cands)

    partial_rows = kernel_apply(
        row_pts, row_sq, col_pts, col_sq, col_dir, signal_scalar, 256
    )
    cand_blocks = []
    width = col_pts.shape[1] // 2
    for k in range(2):
        lo, hi = k * width, (k + 1) * width
        cand_blocks.append(
            lax.optimization_barrier(
                matern_block(
                    row_cands, cand_sq, col_pts[:, lo:hi], col_sq[lo:hi],
                    signal_scalar,
                )
            )
        )
    kernel_row = all_sum(partial_rows, "col", n_col)
    image_row = kernel_row + noise_var[0] * dir_row
    local_sums = jnp.concatenate(
        [jnp.sum(res_row * res_row, axis=1), jnp.sum(dir_row * image_row, axis=1)]
    )
    sums = all_sum(tied(local_sums, w_col), "row", n_row)
    norm_now, curvature = sums[:cols], sums[cols:]
    step_len = norm_now / curvature
    residual_new_row = res_row - step_len[:, None] * image_row

    me_col = lax.axis_index("col")
    own_at = bit_reversed(me_col, n_col.bit_length() - 1) * own
    image_vec = (
        lax.dynamic_slice_in_dim(kernel_row, own_at, own, axis=1)
        + noise_var[0] * direction
    )
    weights_new = weights + step_len[:, None] * direction
    residual_new = residual - step_len[:, None] * image_vec

    w_low_col = (w_col + step_len[:, None] * d_col).astype(jnp.bfloat16)
    partial_fit = None
    for k in range(2):
        lo, hi = k * width, (k + 1) * width
        part = lax.dot_general(
            w_low_col[:, lo:hi], cand_blocks[k], contract_last,
            preferred_element_type=jnp.float32,
        )
        partial_fit = part if partial_fit is None else partial_fit + part
    norm_next = all_sum(
        tied(jnp.sum(residual_new_row * residual_new_row, axis=1), partial_fit),
        "row", n_row,
    )
    direction_new = residual_new + (norm_next / norm_now)[:, None] * direction
    fitted = reduce_scatter_last(partial_fit, "col", n_col)
    cand_fit = cand_prior[None, :] + fitted
    return (weights_new, residual_new, direction_new, cand_fit)


def solution(mesh):
    placed = (
        P(None, ("row", "col")),
        P(None, ("row", "col")),
        P(),
        P(),
        P(),
        P(("row", "col")),
        P(None, ("row", "col")),
        P(None, ("row", "col")),
        P(None, ("row", "col")),
    )
    n_row, n_col = mesh.shape["row"], mesh.shape["col"]

    def body(*args):
        return per_device(*args, n_row=n_row, n_col=n_col)

    return jax.shard_map(
        body,
        mesh=mesh,
        in_specs=placed,
        out_specs=(
            P(None, ("row", "col")),
            P(None, ("row", "col")),
            P(None, ("row", "col")),
            P(None, ("row", "col")),
        ),
        check_vma=False,
    )
```

```python
import math

import jax
import jax.numpy as jnp
from jax import lax
from jax.sharding import PartitionSpec as P


root_five = math.sqrt(5.0)
contract_first = (((0,), (0,)), ((), ()))
contract_last = (((1,), (1,)), ((), ()))


def square_norms(scaled):
    return jnp.sum(jnp.square(scaled.astype(jnp.float32)), axis=0)


def matern_block(row_pts_m2, row_sq, col_pts, col_sq, signal_scalar):
    inner_m2 = lax.dot_general(
        row_pts_m2, col_pts, contract_first, preferred_element_type=jnp.float32
    )
    dist_sq = jnp.maximum(row_sq[:, None] + col_sq[None, :] + inner_m2, 0.0)
    distance = jnp.sqrt(dist_sq)
    kern_vals = (
        signal_scalar
        * (1.0 + root_five * distance + 5.0 / 3.0 * dist_sq)
        * jnp.exp(-root_five * distance)
    )
    return kern_vals.astype(jnp.bfloat16)


def kernel_apply(row_pts_m2, row_sq, col_pts, col_sq, vectors, signal_scalar, block_len):
    feature_count = col_pts.shape[0]
    num_blocks = col_pts.shape[1] // block_len
    pts_blocks = col_pts.reshape(feature_count, num_blocks, block_len).transpose(1, 0, 2)
    sq_blocks = col_sq.reshape(num_blocks, block_len)
    vec_blocks = vectors.reshape(vectors.shape[0], num_blocks, block_len).transpose(1, 0, 2)

    def one_block(total, pieces):
        pts_blk, sq_blk, vec_blk = pieces
        kern_vals = matern_block(row_pts_m2, row_sq, pts_blk, sq_blk, signal_scalar)
        return (
            total
            + lax.dot_general(
                kern_vals, vec_blk, contract_last, preferred_element_type=jnp.float32
            ),
            None,
        )

    start = jnp.zeros((row_pts_m2.shape[1], vectors.shape[0]), jnp.float32)
    result, _ = lax.scan(one_block, start, (pts_blocks, sq_blocks, vec_blocks))
    return result.T


def tied(x, dep):
    x, dep = lax.optimization_barrier((x, dep))
    return x


def xor_perm(size, bit):
    return [(i, i ^ (1 << bit)) for i in range(size)]


def bit_reversed(index, nbits):
    out = 0
    for bit in range(nbits):
        out = out | (((index >> bit) & 1) << (nbits - 1 - bit))
    return out


def gather_last(x, axis_name, size):
    me = lax.axis_index(axis_name)
    buf = x
    for bit in reversed(range(size.bit_length() - 1)):
        recv = lax.ppermute(buf, axis_name, xor_perm(size, bit))
        low = ((me >> bit) & 1) == 0
        buf = jnp.where(
            low, jnp.concatenate([buf, recv], -1), jnp.concatenate([recv, buf], -1)
        )
    return buf


def reduce_scatter_last(x, axis_name, size):
    me = lax.axis_index(axis_name)
    buf = x
    for bit in range(size.bit_length() - 1):
        half = buf.shape[-1] // 2
        lower, upper = buf[..., :half], buf[..., half:]
        low = ((me >> bit) & 1) == 0
        keep = jnp.where(low, lower, upper)
        send = jnp.where(low, upper, lower)
        buf = keep + lax.ppermute(send, axis_name, xor_perm(size, bit))
    return buf


def all_sum(x, axis_name, size):
    for bit in range(size.bit_length() - 1):
        x = x + lax.ppermute(x, axis_name, xor_perm(size, bit))
    return x


def per_device(
    points,
    candidates,
    length_scales,
    signal_var,
    noise_var,
    cand_prior,
    weights,
    residual,
    direction,
    n_row,
    n_col,
):
    scaled = (points / length_scales[:, None]).astype(jnp.bfloat16)
    cand_scaled = (candidates / length_scales[:, None]).astype(jnp.bfloat16)
    signal_scalar = signal_var[0]
    cols, own = direction.shape
    own_cand = cand_scaled.shape[1]
    feats = scaled.shape[0]

    def split(x):
        lo = x - lax.reduce_precision(x, exponent_bits=8, mantissa_bits=7)
        return x.astype(jnp.bfloat16), lo.astype(jnp.bfloat16)

    def join(hi, lo):
        return hi.astype(jnp.float32) + lo.astype(jnp.float32)

    dir_hi, dir_lo = split(direction)
    res_hi, res_lo = split(residual)
    w_hi, w_lo = split(weights)
    cand_rows = own_cand * feats // own
    row_pack = gather_last(
        jnp.concatenate(
            [scaled, cand_scaled.reshape(cand_rows, own), dir_hi, dir_lo, res_hi, res_lo],
            0,
        ),
        "col",
        n_col,
    )
    row_pts = row_pack[:feats]
    row_cands = (
        row_pack[feats:feats + cand_rows]
        .reshape(cand_rows, n_col, own)
        .transpose(1, 0, 2)
        .reshape(n_col, feats, own_cand)
        .transpose(1, 0, 2)
        .reshape(feats, n_col * own_cand)
    )
    at = feats + cand_rows
    dir_row = join(row_pack[at:at + cols], row_pack[at + cols:at + 2 * cols])
    at += 2 * cols
    res_row = join(row_pack[at:at + cols], row_pack[at + cols:at + 2 * cols])
    col_pack = gather_last(
        jnp.concatenate([scaled, dir_hi, dir_lo, w_hi, w_lo], 0), "row", n_row
    )
    col_pts = col_pack[:feats]
    col_dir = col_pack[feats:feats + cols]
    d_col = join(col_dir, col_pack[feats + cols:feats + 2 * cols])
    at = feats + 2 * cols
    w_col = join(col_pack[at:at + cols], col_pack[at + cols:at + 2 * cols])
    row_sq = square_norms(row_pts)
    col_sq = square_norms(col_pts)
    cand_sq = square_norms(row_cands)

    partial_rows = kernel_apply(
        row_pts * jnp.asarray(-2.0, jnp.bfloat16), row_sq, col_pts, col_sq, col_dir, signal_scalar, 256
    )
    cand_blocks = []
    pieces = 4
    width = col_pts.shape[1] // pieces
    for k in range(pieces):
        lo, hi = k * width, (k + 1) * width
        cand_blocks.append(
            lax.optimization_barrier(
                matern_block(
                    row_cands * jnp.asarray(-2.0, jnp.bfloat16), cand_sq, col_pts[:, lo:hi], col_sq[lo:hi],
                    signal_scalar,
                )
            )
        )
    kernel_row = all_sum(partial_rows, "col", n_col)
    image_row = kernel_row + noise_var[0] * dir_row
    local_sums = jnp.concatenate(
        [jnp.sum(res_row * res_row, axis=1), jnp.sum(dir_row * image_row, axis=1)]
    )
    sums = all_sum(tied(local_sums, w_col), "row", n_row)
    norm_now, curvature = sums[:cols], sums[cols:]
    step_len = norm_now / curvature
    residual_new_row = res_row - step_len[:, None] * image_row

    me_col = lax.axis_index("col")
    own_at = bit_reversed(me_col, n_col.bit_length() - 1) * own
    image_vec = (
        lax.dynamic_slice_in_dim(kernel_row, own_at, own, axis=1)
        + noise_var[0] * direction
    )
    weights_new = weights + step_len[:, None] * direction
    residual_new = residual - step_len[:, None] * image_vec

    w_low_col = (w_col + step_len[:, None] * d_col).astype(jnp.bfloat16)
    partial_fit = None
    for k in range(pieces):
        lo, hi = k * width, (k + 1) * width
        part = lax.dot_general(
            w_low_col[:, lo:hi], cand_blocks[k], contract_last,
            preferred_element_type=jnp.float32,
        )
        partial_fit = part if partial_fit is None else partial_fit + part
    norm_next = all_sum(
        tied(jnp.sum(residual_new_row * residual_new_row, axis=1), partial_fit),
        "row", n_row,
    )
    direction_new = residual_new + (norm_next / norm_now)[:, None] * direction
    fitted = reduce_scatter_last(partial_fit, "col", n_col)
    cand_fit = cand_prior[None, :] + fitted
    return (weights_new, residual_new, direction_new, cand_fit)


def solution(mesh):
    placed = (
        P(None, ("row", "col")),
        P(None, ("row", "col")),
        P(),
        P(),
        P(),
        P(("row", "col")),
        P(None, ("row", "col")),
        P(None, ("row", "col")),
        P(None, ("row", "col")),
    )
    n_row, n_col = mesh.shape["row"], mesh.shape["col"]

    def body(*args):
        return per_device(*args, n_row=n_row, n_col=n_col)

    return jax.shard_map(
        body,
        mesh=mesh,
        in_specs=placed,
        out_specs=(
            P(None, ("row", "col")),
            P(None, ("row", "col")),
            P(None, ("row", "col")),
            P(None, ("row", "col")),
        ),
        check_vma=False,
    )
```

```python
import math

import jax
import jax.numpy as jnp
from jax import lax
from jax.sharding import PartitionSpec as P


root_five = math.sqrt(5.0)
exp2_scale = -root_five / math.log(2.0)
contract_first = (((0,), (0,)), ((), ()))
contract_last = (((1,), (1,)), ((), ()))


def square_norms(scaled):
    return jnp.sum(jnp.square(scaled.astype(jnp.float32)), axis=0)


def matern_block(row_pts_m2, row_sq, col_pts, col_sq, signal_scalar):
    inner_m2 = lax.dot_general(
        row_pts_m2, col_pts, contract_first, preferred_element_type=jnp.float32
    )
    dist_sq = jnp.maximum(row_sq[:, None] + col_sq[None, :] + inner_m2, 0.0)
    distance = jnp.sqrt(dist_sq)
    kern_vals = (
        signal_scalar
        * (1.0 + root_five * distance + 5.0 / 3.0 * dist_sq)
        * jnp.exp2(distance * exp2_scale)
    )
    return kern_vals.astype(jnp.bfloat16)


def kernel_apply(row_pts_m2, row_sq, col_pts, col_sq, vectors, signal_scalar, block_len):
    feature_count = col_pts.shape[0]
    num_blocks = col_pts.shape[1] // block_len
    pts_blocks = col_pts.reshape(feature_count, num_blocks, block_len).transpose(1, 0, 2)
    sq_blocks = col_sq.reshape(num_blocks, block_len)
    vec_blocks = vectors.reshape(vectors.shape[0], num_blocks, block_len).transpose(1, 0, 2)

    def one_block(total, pieces):
        pts_blk, sq_blk, vec_blk = pieces
        kern_vals = matern_block(row_pts_m2, row_sq, pts_blk, sq_blk, signal_scalar)
        return (
            total
            + lax.dot_general(
                kern_vals, vec_blk, contract_last, preferred_element_type=jnp.float32
            ),
            None,
        )

    start = jnp.zeros((row_pts_m2.shape[1], vectors.shape[0]), jnp.float32)
    result, _ = lax.scan(one_block, start, (pts_blocks, sq_blocks, vec_blocks))
    return result.T


def tied(x, dep):
    x, dep = lax.optimization_barrier((x, dep))
    return x


def xor_perm(size, bit):
    return [(i, i ^ (1 << bit)) for i in range(size)]


def bit_reversed(index, nbits):
    out = 0
    for bit in range(nbits):
        out = out | (((index >> bit) & 1) << (nbits - 1 - bit))
    return out


def gather_last(x, axis_name, size):
    me = lax.axis_index(axis_name)
    buf = x
    for bit in reversed(range(size.bit_length() - 1)):
        recv = lax.ppermute(buf, axis_name, xor_perm(size, bit))
        low = ((me >> bit) & 1) == 0
        buf = jnp.where(
            low, jnp.concatenate([buf, recv], -1), jnp.concatenate([recv, buf], -1)
        )
    return buf


def reduce_scatter_last(x, axis_name, size):
    me = lax.axis_index(axis_name)
    buf = x
    for bit in range(size.bit_length() - 1):
        half = buf.shape[-1] // 2
        lower, upper = buf[..., :half], buf[..., half:]
        low = ((me >> bit) & 1) == 0
        keep = jnp.where(low, lower, upper)
        send = jnp.where(low, upper, lower)
        buf = keep + lax.ppermute(send, axis_name, xor_perm(size, bit))
    return buf


def all_sum(x, axis_name, size):
    for bit in range(size.bit_length() - 1):
        x = x + lax.ppermute(x, axis_name, xor_perm(size, bit))
    return x


def per_device(
    points,
    candidates,
    length_scales,
    signal_var,
    noise_var,
    cand_prior,
    weights,
    residual,
    direction,
    n_row,
    n_col,
):
    scaled = (points / length_scales[:, None]).astype(jnp.bfloat16)
    cand_scaled = (candidates / length_scales[:, None]).astype(jnp.bfloat16)
    signal_scalar = signal_var[0]
    cols, own = direction.shape
    own_cand = cand_scaled.shape[1]
    feats = scaled.shape[0]

    def split(x):
        lo = x - lax.reduce_precision(x, exponent_bits=8, mantissa_bits=7)
        return x.astype(jnp.bfloat16), lo.astype(jnp.bfloat16)

    def join(hi, lo):
        return hi.astype(jnp.float32) + lo.astype(jnp.float32)

    dir_hi, dir_lo = split(direction)
    res_hi, res_lo = split(residual)
    w_hi, w_lo = split(weights)
    cand_rows = own_cand * feats // own
    row_pack = gather_last(
        jnp.concatenate(
            [scaled, cand_scaled.reshape(cand_rows, own), dir_hi, dir_lo, res_hi, res_lo],
            0,
        ),
        "col",
        n_col,
    )
    row_pts = row_pack[:feats]
    row_cands = (
        row_pack[feats:feats + cand_rows]
        .reshape(cand_rows, n_col, own)
        .transpose(1, 0, 2)
        .reshape(n_col, feats, own_cand)
        .transpose(1, 0, 2)
        .reshape(feats, n_col * own_cand)
    )
    at = feats + cand_rows
    dir_row = join(row_pack[at:at + cols], row_pack[at + cols:at + 2 * cols])
    at += 2 * cols
    res_row = join(row_pack[at:at + cols], row_pack[at + cols:at + 2 * cols])
    col_pack = gather_last(
        jnp.concatenate([scaled, dir_hi, dir_lo, w_hi, w_lo], 0), "row", n_row
    )
    col_pts = col_pack[:feats]
    col_dir = col_pack[feats:feats + cols]
    d_col = join(col_dir, col_pack[feats + cols:feats + 2 * cols])
    at = feats + 2 * cols
    w_col = join(col_pack[at:at + cols], col_pack[at + cols:at + 2 * cols])
    row_sq = square_norms(row_pts)
    col_sq = square_norms(col_pts)
    cand_sq = square_norms(row_cands)

    partial_rows = kernel_apply(
        row_pts * jnp.asarray(-2.0, jnp.bfloat16), row_sq, col_pts, col_sq, col_dir, signal_scalar, 256
    )
    cand_blocks = []
    width = col_pts.shape[1] // 2
    for k in range(2):
        lo, hi = k * width, (k + 1) * width
        cand_blocks.append(
            lax.optimization_barrier(
                matern_block(
                    row_cands * jnp.asarray(-2.0, jnp.bfloat16), cand_sq, col_pts[:, lo:hi], col_sq[lo:hi],
                    signal_scalar,
                )
            )
        )
    kernel_row = all_sum(partial_rows, "col", n_col)
    image_row = kernel_row + noise_var[0] * dir_row
    local_sums = jnp.concatenate(
        [jnp.sum(res_row * res_row, axis=1), jnp.sum(dir_row * image_row, axis=1)]
    )
    sums = all_sum(tied(local_sums, w_col), "row", n_row)
    norm_now, curvature = sums[:cols], sums[cols:]
    step_len = norm_now / curvature
    residual_new_row = res_row - step_len[:, None] * image_row

    me_col = lax.axis_index("col")
    own_at = bit_reversed(me_col, n_col.bit_length() - 1) * own
    image_vec = (
        lax.dynamic_slice_in_dim(kernel_row, own_at, own, axis=1)
        + noise_var[0] * direction
    )
    weights_new = weights + step_len[:, None] * direction
    residual_new = residual - step_len[:, None] * image_vec

    w_low_col = (w_col + step_len[:, None] * d_col).astype(jnp.bfloat16)
    partial_fit = None
    for k in range(2):
        lo, hi = k * width, (k + 1) * width
        part = lax.dot_general(
            w_low_col[:, lo:hi], cand_blocks[k], contract_last,
            preferred_element_type=jnp.float32,
        )
        partial_fit = part if partial_fit is None else partial_fit + part
    norm_next = all_sum(
        tied(jnp.sum(residual_new_row * residual_new_row, axis=1), partial_fit),
        "row", n_row,
    )
    direction_new = residual_new + (norm_next / norm_now)[:, None] * direction
    fitted = reduce_scatter_last(partial_fit, "col", n_col)
    cand_fit = cand_prior[None, :] + fitted
    return (weights_new, residual_new, direction_new, cand_fit)


def solution(mesh):
    placed = (
        P(None, ("row", "col")),
        P(None, ("row", "col")),
        P(),
        P(),
        P(),
        P(("row", "col")),
        P(None, ("row", "col")),
        P(None, ("row", "col")),
        P(None, ("row", "col")),
    )
    n_row, n_col = mesh.shape["row"], mesh.shape["col"]

    def body(*args):
        return per_device(*args, n_row=n_row, n_col=n_col)

    return jax.shard_map(
        body,
        mesh=mesh,
        in_specs=placed,
        out_specs=(
            P(None, ("row", "col")),
            P(None, ("row", "col")),
            P(None, ("row", "col")),
            P(None, ("row", "col")),
        ),
        check_vma=False,
    )
```

```python
import math

import jax
import jax.numpy as jnp
from jax import lax
from jax.sharding import PartitionSpec as P


root_five = math.sqrt(5.0)
contract_first = (((0,), (0,)), ((), ()))
contract_last = (((1,), (1,)), ((), ()))


def square_norms(scaled):
    return jnp.sum(jnp.square(scaled.astype(jnp.float32)), axis=0)


def matern_block(row_pts_m2, row_sq, col_pts, col_sq, signal_scalar):
    inner_m2 = lax.dot_general(
        row_pts_m2, col_pts, contract_first, preferred_element_type=jnp.float32
    )
    dist_sq = jnp.maximum(row_sq[:, None] + col_sq[None, :] + inner_m2, 0.0)
    distance = jnp.sqrt(dist_sq)
    kern_vals = (
        signal_scalar
        * (1.0 + root_five * distance + 5.0 / 3.0 * dist_sq)
        * jnp.exp(-root_five * distance)
    )
    return kern_vals.astype(jnp.bfloat16)


def kernel_apply(row_pts_m2, row_sq, col_pts, col_sq, vectors, signal_scalar, block_len):
    feature_count = col_pts.shape[0]
    num_blocks = col_pts.shape[1] // block_len
    pts_blocks = col_pts.reshape(feature_count, num_blocks, block_len).transpose(1, 0, 2)
    sq_blocks = col_sq.reshape(num_blocks, block_len)
    vec_blocks = vectors.reshape(vectors.shape[0], num_blocks, block_len).transpose(1, 0, 2)

    def one_block(total, pieces):
        pts_blk, sq_blk, vec_blk = pieces
        kern_vals = matern_block(row_pts_m2, row_sq, pts_blk, sq_blk, signal_scalar)
        return (
            total
            + lax.dot_general(
                kern_vals, vec_blk, contract_last, preferred_element_type=jnp.float32
            ),
            None,
        )

    start = jnp.zeros((row_pts_m2.shape[1], vectors.shape[0]), jnp.float32)
    result, _ = lax.scan(one_block, start, (pts_blocks, sq_blocks, vec_blocks))
    return result.T


def tied(x, dep):
    x, dep = lax.optimization_barrier((x, dep))
    return x


def xor_perm(size, bit):
    return [(i, i ^ (1 << bit)) for i in range(size)]


def bit_reversed(index, nbits):
    out = 0
    for bit in range(nbits):
        out = out | (((index >> bit) & 1) << (nbits - 1 - bit))
    return out


def gather_last(x, axis_name, size):
    me = lax.axis_index(axis_name)
    buf = x
    for bit in reversed(range(size.bit_length() - 1)):
        recv = lax.ppermute(buf, axis_name, xor_perm(size, bit))
        low = ((me >> bit) & 1) == 0
        buf = jnp.where(
            low, jnp.concatenate([buf, recv], -1), jnp.concatenate([recv, buf], -1)
        )
    return buf


def all_sum(x, axis_name, size):
    for bit in range(size.bit_length() - 1):
        x = x + lax.ppermute(x, axis_name, xor_perm(size, bit))
    return x


def tail_sums(fit, local, axis_rs, axis_ar, size_rs, size_ar):
    me = lax.axis_index(axis_rs)
    buf, x = fit, local
    for bit in range(size_rs.bit_length() - 1):
        half = buf.shape[-1] // 2
        lower, upper = buf[..., :half], buf[..., half:]
        low = ((me >> bit) & 1) == 0
        keep = jnp.where(low, lower, upper)
        send = jnp.where(low, upper, lower)
        send, x = lax.optimization_barrier((send, x))
        got = lax.ppermute(send, axis_rs, xor_perm(size_rs, bit))
        x = x + lax.ppermute(x, axis_ar, xor_perm(size_ar, bit))
        buf = keep + got
    return buf, x


def per_device(
    points,
    candidates,
    length_scales,
    signal_var,
    noise_var,
    cand_prior,
    weights,
    residual,
    direction,
    n_row,
    n_col,
):
    scaled = (points / length_scales[:, None]).astype(jnp.bfloat16)
    cand_scaled = (candidates / length_scales[:, None]).astype(jnp.bfloat16)
    signal_scalar = signal_var[0]
    cols, own = direction.shape
    own_cand = cand_scaled.shape[1]
    feats = scaled.shape[0]

    def split(x):
        lo = x - lax.reduce_precision(x, exponent_bits=8, mantissa_bits=7)
        return x.astype(jnp.bfloat16), lo.astype(jnp.bfloat16)

    def join(hi, lo):
        return hi.astype(jnp.float32) + lo.astype(jnp.float32)

    dir_hi, dir_lo = split(direction)
    res_hi, res_lo = split(residual)
    w_hi, w_lo = split(weights)
    cand_rows = own_cand * feats // own
    row_pack = gather_last(
        jnp.concatenate(
            [scaled, cand_scaled.reshape(cand_rows, own), dir_hi, dir_lo, res_hi, res_lo],
            0,
        ),
        "col",
        n_col,
    )
    row_pts = row_pack[:feats]
    row_cands = (
        row_pack[feats:feats + cand_rows]
        .reshape(cand_rows, n_col, own)
        .transpose(1, 0, 2)
        .reshape(n_col, feats, own_cand)
        .transpose(1, 0, 2)
        .reshape(feats, n_col * own_cand)
    )
    at = feats + cand_rows
    dir_row = join(row_pack[at:at + cols], row_pack[at + cols:at + 2 * cols])
    at += 2 * cols
    res_row = join(row_pack[at:at + cols], row_pack[at + cols:at + 2 * cols])
    col_pack = gather_last(
        jnp.concatenate([scaled, dir_hi, dir_lo, w_hi, w_lo], 0), "row", n_row
    )
    col_pts = col_pack[:feats]
    col_dir = col_pack[feats:feats + cols]
    d_col = join(col_dir, col_pack[feats + cols:feats + 2 * cols])
    at = feats + 2 * cols
    w_col = join(col_pack[at:at + cols], col_pack[at + cols:at + 2 * cols])
    row_sq = square_norms(row_pts)
    col_sq = square_norms(col_pts)
    cand_sq = square_norms(row_cands)

    partial_rows = kernel_apply(
        row_pts * jnp.asarray(-2.0, jnp.bfloat16), row_sq, col_pts, col_sq, col_dir, signal_scalar, 256
    )
    cand_blocks = []
    width = col_pts.shape[1] // 2
    for k in range(2):
        lo, hi = k * width, (k + 1) * width
        cand_blocks.append(
            lax.optimization_barrier(
                matern_block(
                    row_cands * jnp.asarray(-2.0, jnp.bfloat16), cand_sq, col_pts[:, lo:hi], col_sq[lo:hi],
                    signal_scalar,
                )
            )
        )
    kernel_row = all_sum(partial_rows, "col", n_col)
    image_row = kernel_row + noise_var[0] * dir_row
    local_sums = jnp.concatenate(
        [jnp.sum(res_row * res_row, axis=1), jnp.sum(dir_row * image_row, axis=1)]
    )
    sums = all_sum(tied(local_sums, w_col), "row", n_row)
    norm_now, curvature = sums[:cols], sums[cols:]
    step_len = norm_now / curvature
    residual_new_row = res_row - step_len[:, None] * image_row

    me_col = lax.axis_index("col")
    own_at = bit_reversed(me_col, n_col.bit_length() - 1) * own
    image_vec = (
        lax.dynamic_slice_in_dim(kernel_row, own_at, own, axis=1)
        + noise_var[0] * direction
    )
    weights_new = weights + step_len[:, None] * direction
    residual_new = residual - step_len[:, None] * image_vec

    w_low_col = (w_col + step_len[:, None] * d_col).astype(jnp.bfloat16)
    partial_fit = None
    for k in range(2):
        lo, hi = k * width, (k + 1) * width
        part = lax.dot_general(
            w_low_col[:, lo:hi], cand_blocks[k], contract_last,
            preferred_element_type=jnp.float32,
        )
        partial_fit = part if partial_fit is None else partial_fit + part
    fitted, norm_next = tail_sums(
        partial_fit, jnp.sum(residual_new_row * residual_new_row, axis=1),
        "col", "row", n_col, n_row,
    )
    direction_new = residual_new + (norm_next / norm_now)[:, None] * direction
    cand_fit = cand_prior[None, :] + fitted
    return (weights_new, residual_new, direction_new, cand_fit)


def solution(mesh):
    placed = (
        P(None, ("row", "col")),
        P(None, ("row", "col")),
        P(),
        P(),
        P(),
        P(("row", "col")),
        P(None, ("row", "col")),
        P(None, ("row", "col")),
        P(None, ("row", "col")),
    )
    n_row, n_col = mesh.shape["row"], mesh.shape["col"]

    def body(*args):
        return per_device(*args, n_row=n_row, n_col=n_col)

    return jax.shard_map(
        body,
        mesh=mesh,
        in_specs=placed,
        out_specs=(
            P(None, ("row", "col")),
            P(None, ("row", "col")),
            P(None, ("row", "col")),
            P(None, ("row", "col")),
        ),
        check_vma=False,
    )
```

```python
import math

import jax
import jax.numpy as jnp
from jax import lax
from jax.sharding import PartitionSpec as P


root_five = math.sqrt(5.0)
contract_first = (((0,), (0,)), ((), ()))
contract_last = (((1,), (1,)), ((), ()))


def square_norms(scaled):
    return jnp.sum(jnp.square(scaled.astype(jnp.float32)), axis=0)


def matern_block(row_pts_m2, row_sq, col_pts, col_sq, signal_scalar):
    inner_m2 = lax.dot_general(
        row_pts_m2, col_pts, contract_first, preferred_element_type=jnp.float32
    )
    dist_sq = jnp.maximum(row_sq[:, None] + col_sq[None, :] + inner_m2, 0.0)
    distance = jnp.sqrt(dist_sq)
    kern_vals = (
        signal_scalar
        * (1.0 + root_five * distance + 5.0 / 3.0 * dist_sq)
        * jnp.exp(-root_five * distance)
    )
    return kern_vals.astype(jnp.bfloat16)


def kernel_apply(row_pts_m2, row_sq, col_pts, col_sq, vectors, signal_scalar, block_len):
    feature_count = col_pts.shape[0]
    num_blocks = col_pts.shape[1] // block_len
    pts_blocks = col_pts.reshape(feature_count, num_blocks, block_len).transpose(1, 0, 2)
    sq_blocks = col_sq.reshape(num_blocks, block_len)
    vec_blocks = vectors.reshape(vectors.shape[0], num_blocks, block_len).transpose(1, 0, 2)

    def one_block(total, pieces):
        pts_blk, sq_blk, vec_blk = pieces
        kern_vals = matern_block(row_pts_m2, row_sq, pts_blk, sq_blk, signal_scalar)
        return (
            total
            + lax.dot_general(
                kern_vals, vec_blk, contract_last, preferred_element_type=jnp.float32
            ),
            None,
        )

    start = jnp.zeros((row_pts_m2.shape[1], vectors.shape[0]), jnp.float32)
    result, _ = lax.scan(one_block, start, (pts_blocks, sq_blocks, vec_blocks))
    return result.T


def xor_perm(size, bit):
    return [(i, i ^ (1 << bit)) for i in range(size)]


def bit_reversed(index, nbits):
    out = 0
    for bit in range(nbits):
        out = out | (((index >> bit) & 1) << (nbits - 1 - bit))
    return out


def gather_last(x, axis_name, size):
    me = lax.axis_index(axis_name)
    buf = x
    for bit in reversed(range(size.bit_length() - 1)):
        recv = lax.ppermute(buf, axis_name, xor_perm(size, bit))
        low = ((me >> bit) & 1) == 0
        buf = jnp.where(
            low, jnp.concatenate([buf, recv], -1), jnp.concatenate([recv, buf], -1)
        )
    return buf


def col_sum_with_grid(rows, sums, n_row, n_col):
    cols = rows.shape[0]
    extra = sums.shape[0] // cols
    for bit in range(n_col.bit_length() - 1):
        packed = jnp.concatenate([rows, sums.reshape(cols, extra)], 1)
        got = lax.ppermute(packed, "col", xor_perm(n_col, bit))
        step = 1 << bit
        diag = [
            (r * n_col + c, (r ^ step) * n_col + (c ^ step))
            for r in range(n_row)
            for c in range(n_col)
        ]
        from_row = lax.ppermute(sums, "row", xor_perm(n_row, bit))
        from_diag = lax.ppermute(sums, ("row", "col"), diag)
        rows = rows + got[:, : rows.shape[1]]
        from_col = got[:, rows.shape[1]:].reshape(-1)
        sums = (sums + from_col) + (from_row + from_diag)
    return rows, sums


def tail_sums(fit, local, axis_rs, axis_ar, size_rs, size_ar):
    me = lax.axis_index(axis_rs)
    buf, x = fit, local
    for bit in range(size_rs.bit_length() - 1):
        half = buf.shape[-1] // 2
        lower, upper = buf[..., :half], buf[..., half:]
        low = ((me >> bit) & 1) == 0
        keep = jnp.where(low, lower, upper)
        send = jnp.where(low, upper, lower)
        send, x = lax.optimization_barrier((send, x))
        got = lax.ppermute(send, axis_rs, xor_perm(size_rs, bit))
        x = x + lax.ppermute(x, axis_ar, xor_perm(size_ar, bit))
        buf = keep + got
    return buf, x


def per_device(
    points,
    candidates,
    length_scales,
    signal_var,
    noise_var,
    cand_prior,
    weights,
    residual,
    direction,
    n_row,
    n_col,
):
    scaled = (points / length_scales[:, None]).astype(jnp.bfloat16)
    cand_scaled = (candidates / length_scales[:, None]).astype(jnp.bfloat16)
    signal_scalar = signal_var[0]
    cols, own = direction.shape
    own_cand = cand_scaled.shape[1]
    feats = scaled.shape[0]

    def split(x):
        lo = x - lax.reduce_precision(x, exponent_bits=8, mantissa_bits=7)
        return x.astype(jnp.bfloat16), lo.astype(jnp.bfloat16)

    def join(hi, lo):
        return hi.astype(jnp.float32) + lo.astype(jnp.float32)

    dir_hi, dir_lo = split(direction)
    res_hi, res_lo = split(residual)
    w_hi, w_lo = split(weights)
    cand_rows = own_cand * feats // own
    row_pack = gather_last(
        jnp.concatenate(
            [scaled, cand_scaled.reshape(cand_rows, own), dir_hi, dir_lo, res_hi, res_lo],
            0,
        ),
        "col",
        n_col,
    )
    row_pts = row_pack[:feats]
    row_cands = (
        row_pack[feats:feats + cand_rows]
        .reshape(cand_rows, n_col, own)
        .transpose(1, 0, 2)
        .reshape(n_col, feats, own_cand)
        .transpose(1, 0, 2)
        .reshape(feats, n_col * own_cand)
    )
    at = feats + cand_rows
    dir_row = join(row_pack[at:at + cols], row_pack[at + cols:at + 2 * cols])
    at += 2 * cols
    res_row = join(row_pack[at:at + cols], row_pack[at + cols:at + 2 * cols])
    col_pack = gather_last(
        jnp.concatenate([scaled, dir_hi, dir_lo, w_hi, w_lo], 0), "row", n_row
    )
    col_pts = col_pack[:feats]
    col_dir = col_pack[feats:feats + cols]
    d_col = join(col_dir, col_pack[feats + cols:feats + 2 * cols])
    at = feats + 2 * cols
    w_col = join(col_pack[at:at + cols], col_pack[at + cols:at + 2 * cols])
    row_sq = square_norms(row_pts)
    col_sq = square_norms(col_pts)
    cand_sq = square_norms(row_cands)

    partial_rows = kernel_apply(
        row_pts * jnp.asarray(-2.0, jnp.bfloat16), row_sq, col_pts, col_sq, col_dir, signal_scalar, 256
    )
    cand_blocks = []
    width = col_pts.shape[1] // 2
    for k in range(2):
        lo, hi = k * width, (k + 1) * width
        cand_blocks.append(
            lax.optimization_barrier(
                matern_block(
                    row_cands * jnp.asarray(-2.0, jnp.bfloat16), cand_sq, col_pts[:, lo:hi], col_sq[lo:hi],
                    signal_scalar,
                )
            )
        )
    noise = noise_var[0]
    local_sums = jnp.concatenate(
        [
            jnp.sum(residual * residual, axis=1),
            jnp.sum(dir_row * partial_rows, axis=1)
            + noise * jnp.sum(direction * direction, axis=1),
        ]
    )
    kernel_row, sums = col_sum_with_grid(partial_rows, local_sums, n_row, n_col)
    image_row = kernel_row + noise * dir_row
    norm_now, curvature = sums[:cols], sums[cols:]
    step_len = norm_now / curvature
    residual_new_row = res_row - step_len[:, None] * image_row

    me_col = lax.axis_index("col")
    own_at = bit_reversed(me_col, n_col.bit_length() - 1) * own
    image_vec = (
        lax.dynamic_slice_in_dim(kernel_row, own_at, own, axis=1)
        + noise_var[0] * direction
    )
    weights_new = weights + step_len[:, None] * direction
    residual_new = residual - step_len[:, None] * image_vec

    w_low_col = (w_col + step_len[:, None] * d_col).astype(jnp.bfloat16)
    partial_fit = None
    for k in range(2):
        lo, hi = k * width, (k + 1) * width
        part = lax.dot_general(
            w_low_col[:, lo:hi], cand_blocks[k], contract_last,
            preferred_element_type=jnp.float32,
        )
        partial_fit = part if partial_fit is None else partial_fit + part
    fitted, norm_next = tail_sums(
        partial_fit, jnp.sum(residual_new_row * residual_new_row, axis=1),
        "col", "row", n_col, n_row,
    )
    direction_new = residual_new + (norm_next / norm_now)[:, None] * direction
    cand_fit = cand_prior[None, :] + fitted
    return (weights_new, residual_new, direction_new, cand_fit)


def solution(mesh):
    placed = (
        P(None, ("row", "col")),
        P(None, ("row", "col")),
        P(),
        P(),
        P(),
        P(("row", "col")),
        P(None, ("row", "col")),
        P(None, ("row", "col")),
        P(None, ("row", "col")),
    )
    n_row, n_col = mesh.shape["row"], mesh.shape["col"]

    def body(*args):
        return per_device(*args, n_row=n_row, n_col=n_col)

    return jax.shard_map(
        body,
        mesh=mesh,
        in_specs=placed,
        out_specs=(
            P(None, ("row", "col")),
            P(None, ("row", "col")),
            P(None, ("row", "col")),
            P(None, ("row", "col")),
        ),
        check_vma=False,
    )
```

```python
import math

import jax
import jax.numpy as jnp
from jax import lax
from jax.sharding import PartitionSpec as P


root_five = math.sqrt(5.0)
contract_first = (((0,), (0,)), ((), ()))
contract_last = (((1,), (1,)), ((), ()))


def square_norms(scaled):
    return jnp.sum(jnp.square(scaled.astype(jnp.float32)), axis=0)


def matern_block(row_pts_m2, row_sq, col_pts, col_sq, signal_scalar):
    inner_m2 = lax.dot_general(
        row_pts_m2, col_pts, contract_first, preferred_element_type=jnp.float32
    )
    dist_sq = jnp.maximum(row_sq[:, None] + col_sq[None, :] + inner_m2, 0.0)
    distance = jnp.sqrt(dist_sq)
    kern_vals = (
        signal_scalar
        * (1.0 + root_five * distance + 5.0 / 3.0 * dist_sq)
        * jnp.exp(-root_five * distance)
    )
    return kern_vals.astype(jnp.bfloat16)


def kernel_apply(row_pts_m2, row_sq, col_pts, col_sq, vectors, signal_scalar, block_len):
    feature_count = col_pts.shape[0]
    num_blocks = col_pts.shape[1] // block_len
    pts_blocks = col_pts.reshape(feature_count, num_blocks, block_len).transpose(1, 0, 2)
    sq_blocks = col_sq.reshape(num_blocks, block_len)
    vec_blocks = vectors.reshape(vectors.shape[0], num_blocks, block_len).transpose(1, 0, 2)

    def one_block(total, pieces):
        pts_blk, sq_blk, vec_blk = pieces
        kern_vals = matern_block(row_pts_m2, row_sq, pts_blk, sq_blk, signal_scalar)
        return (
            total
            + lax.dot_general(
                kern_vals, vec_blk, contract_last, preferred_element_type=jnp.float32
            ),
            None,
        )

    start = jnp.zeros((row_pts_m2.shape[1], vectors.shape[0]), jnp.float32)
    result, _ = lax.scan(one_block, start, (pts_blocks, sq_blocks, vec_blocks))
    return result.T


def xor_perm(size, bit):
    return [(i, i ^ (1 << bit)) for i in range(size)]


def bit_reversed(index, nbits):
    out = 0
    for bit in range(nbits):
        out = out | (((index >> bit) & 1) << (nbits - 1 - bit))
    return out


def gather_last(x, axis_name, size):
    me = lax.axis_index(axis_name)
    buf = x
    for bit in reversed(range(size.bit_length() - 1)):
        recv = lax.ppermute(buf, axis_name, xor_perm(size, bit))
        low = ((me >> bit) & 1) == 0
        buf = jnp.where(
            low, jnp.concatenate([buf, recv], -1), jnp.concatenate([recv, buf], -1)
        )
    return buf


def col_sum_with_grid(rows, sums, n_row, n_col):
    cols = rows.shape[0]
    extra = sums.shape[0] // cols
    for bit in range(n_col.bit_length() - 1):
        packed = jnp.concatenate([rows, sums.reshape(cols, extra)], 1)
        got = lax.ppermute(packed, "col", xor_perm(n_col, bit))
        step = 1 << bit
        diag = [
            (r * n_col + c, (r ^ step) * n_col + (c ^ step))
            for r in range(n_row)
            for c in range(n_col)
        ]
        from_row = lax.ppermute(sums, "row", xor_perm(n_row, bit))
        from_diag = lax.ppermute(sums, ("row", "col"), diag)
        rows = rows + got[:, : rows.shape[1]]
        from_col = got[:, rows.shape[1]:].reshape(-1)
        sums = (sums + from_col) + (from_row + from_diag)
    return rows, sums


def tail_sums(fit, local, axis_rs, axis_ar, size_rs, size_ar):
    me = lax.axis_index(axis_rs)
    buf, x = fit, local
    for bit in range(size_rs.bit_length() - 1):
        half = buf.shape[-1] // 2
        lower, upper = buf[..., :half], buf[..., half:]
        low = ((me >> bit) & 1) == 0
        keep = jnp.where(low, lower, upper)
        send = jnp.where(low, upper, lower)
        send, x = lax.optimization_barrier((send, x))
        got = lax.ppermute(send, axis_rs, xor_perm(size_rs, bit))
        x = x + lax.ppermute(x, axis_ar, xor_perm(size_ar, bit))
        buf = keep + got
    return buf, x


def per_device(
    points,
    candidates,
    length_scales,
    signal_var,
    noise_var,
    cand_prior,
    weights,
    residual,
    direction,
    n_row,
    n_col,
):
    scaled = (points / length_scales[:, None]).astype(jnp.bfloat16)
    cand_scaled = (candidates / length_scales[:, None]).astype(jnp.bfloat16)
    signal_scalar = signal_var[0]
    cols, own = direction.shape
    own_cand = cand_scaled.shape[1]
    feats = scaled.shape[0]

    def split(x):
        lo = x - lax.reduce_precision(x, exponent_bits=8, mantissa_bits=7)
        return x.astype(jnp.bfloat16), lo.astype(jnp.bfloat16)

    def join(hi, lo):
        return hi.astype(jnp.float32) + lo.astype(jnp.float32)

    dir_hi, dir_lo = split(direction)
    res_hi, res_lo = split(residual)
    w_hi, w_lo = split(weights)
    cand_rows = own_cand * feats // own
    row_pack = gather_last(
        jnp.concatenate(
            [scaled, cand_scaled.reshape(cand_rows, own), dir_hi, dir_lo, res_hi, res_lo],
            0,
        ),
        "col",
        n_col,
    )
    row_pts = row_pack[:feats]
    row_cands = (
        row_pack[feats:feats + cand_rows]
        .reshape(cand_rows, n_col, own)
        .transpose(1, 0, 2)
        .reshape(n_col, feats, own_cand)
        .transpose(1, 0, 2)
        .reshape(feats, n_col * own_cand)
    )
    at = feats + cand_rows
    dir_row = join(row_pack[at:at + cols], row_pack[at + cols:at + 2 * cols])
    at += 2 * cols
    res_row = join(row_pack[at:at + cols], row_pack[at + cols:at + 2 * cols])
    col_pack = gather_last(
        jnp.concatenate([scaled, dir_hi, dir_lo, w_hi, w_lo], 0), "row", n_row
    )
    col_pts = col_pack[:feats]
    col_dir = col_pack[feats:feats + cols]
    d_col = join(col_dir, col_pack[feats + cols:feats + 2 * cols])
    at = feats + 2 * cols
    w_col = join(col_pack[at:at + cols], col_pack[at + cols:at + 2 * cols])
    row_sq = square_norms(row_pts)
    col_sq = square_norms(col_pts)
    cand_sq = square_norms(row_cands)

    partial_rows = kernel_apply(
        row_pts * jnp.asarray(-2.0, jnp.bfloat16), row_sq, col_pts, col_sq, col_dir, signal_scalar, 256
    )
    cand_blocks = []
    pieces = 4
    width = col_pts.shape[1] // pieces
    for k in range(pieces):
        lo, hi = k * width, (k + 1) * width
        cand_blocks.append(
            lax.optimization_barrier(
                matern_block(
                    row_cands * jnp.asarray(-2.0, jnp.bfloat16), cand_sq, col_pts[:, lo:hi], col_sq[lo:hi],
                    signal_scalar,
                )
            )
        )
    noise = noise_var[0]
    local_sums = jnp.concatenate(
        [
            jnp.sum(residual * residual, axis=1),
            jnp.sum(dir_row * partial_rows, axis=1)
            + noise * jnp.sum(direction * direction, axis=1),
        ]
    )
    kernel_row, sums = col_sum_with_grid(partial_rows, local_sums, n_row, n_col)
    image_row = kernel_row + noise * dir_row
    norm_now, curvature = sums[:cols], sums[cols:]
    step_len = norm_now / curvature
    residual_new_row = res_row - step_len[:, None] * image_row

    me_col = lax.axis_index("col")
    own_at = bit_reversed(me_col, n_col.bit_length() - 1) * own
    image_vec = (
        lax.dynamic_slice_in_dim(kernel_row, own_at, own, axis=1)
        + noise_var[0] * direction
    )
    weights_new = weights + step_len[:, None] * direction
    residual_new = residual - step_len[:, None] * image_vec

    w_low_col = (w_col + step_len[:, None] * d_col).astype(jnp.bfloat16)
    partial_fit = None
    for k in range(pieces):
        lo, hi = k * width, (k + 1) * width
        part = lax.dot_general(
            w_low_col[:, lo:hi], cand_blocks[k], contract_last,
            preferred_element_type=jnp.float32,
        )
        partial_fit = part if partial_fit is None else partial_fit + part
    fitted, norm_next = tail_sums(
        partial_fit, jnp.sum(residual_new_row * residual_new_row, axis=1),
        "col", "row", n_col, n_row,
    )
    direction_new = residual_new + (norm_next / norm_now)[:, None] * direction
    cand_fit = cand_prior[None, :] + fitted
    return (weights_new, residual_new, direction_new, cand_fit)


def solution(mesh):
    placed = (
        P(None, ("row", "col")),
        P(None, ("row", "col")),
        P(),
        P(),
        P(),
        P(("row", "col")),
        P(None, ("row", "col")),
        P(None, ("row", "col")),
        P(None, ("row", "col")),
    )
    n_row, n_col = mesh.shape["row"], mesh.shape["col"]

    def body(*args):
        return per_device(*args, n_row=n_row, n_col=n_col)

    return jax.shard_map(
        body,
        mesh=mesh,
        in_specs=placed,
        out_specs=(
            P(None, ("row", "col")),
            P(None, ("row", "col")),
            P(None, ("row", "col")),
            P(None, ("row", "col")),
        ),
        check_vma=False,
    )
```
